128 devices in a mesh: seq: 32 (over x, z, y_lo), dp: 4 (over y_hi, core).
Axes of the slice: x: 4, y: 4 (y_hi: 2, y_lo: 2; y = y_hi * 2 + y_lo), z: 4, core: 2. Of those that a mesh axis runs over, the one named last changes fastest.
Arguments:
- signal: bfloat16 [65536, 128], P(('seq', 'dp')), may hold values from -6 to 6
- filter_param: bfloat16 [65536, 128], P(('seq', 'dp')), may hold values from -6 to 6
- skip_gain: float32 [128], replicated, may hold values from 0.5 to 1.5
- out_grad: bfloat16 [65536, 128], P(('seq', 'dp')), may hold values from -6 to 6
Outputs:
- conv_out: bfloat16 [65536, 128], P(('seq', 'dp'))
- input_grad: bfloat16 [65536, 128], P(('seq', 'dp'))
- filter_grad: float32 [65536, 128], P(('seq', 'dp'))
The draws below stay inside these ranges and needn't reach their ends.
All inputs are finite; a program needn't handle non-finite values.
Results may differ from the reference program's by a relative error of at most 0.001.
Values may be sent and summed in bfloat16 or wider, within the bound.
No kernel may reach another device: no remote copies, remote signals or barrier semaphores. Data moves between devices by JAX's collectives and lax.ppermute only.
A program may use at most 64 MiB of HBM per device.

```python
import math
import jax
import jax.numpy as jnp

CHANNELS = 128
LENGTH = 65536


def shard_levels(key, shape, shards, low, high):
    def one(axis_at, blocks):
        heights = jax.random.uniform(jax.random.fold_in(jax.random.fold_in(key, 6), axis_at), (blocks,), jnp.float32, low / len(shards), high / len(shards))
        return jnp.repeat(jnp.exp(heights), shape[axis_at] // blocks).reshape((-1,) + (1,) * (len(shape) - axis_at - 1))

    level = one(*shards[0])
    for cut in shards[1:]:
        level = level * one(*cut)
    return level


def normal_values(stream_key, dims, scale, limit, pieces=(), held_as=jnp.bfloat16):
    level = shard_levels(stream_key, dims, pieces, -0.22, 0.18) if pieces else 1.0
    drawn = jax.random.normal(stream_key, dims, jnp.float32) * scale * level
    return jnp.minimum(jnp.maximum(drawn, -limit), limit).astype(held_as)


def setup_inputs(seed: int = 0) -> dict:
    key_of = jax.random.split(jax.random.key(seed), 5)
    signal = normal_values(key_of[0], (LENGTH, CHANNELS), 1.0, 6.0, ((0, 128),))
    filter_param = normal_values(key_of[1], (LENGTH, CHANNELS), 1.0, 6.0, ((0, 128),))
    skip_gain = jnp.clip(jax.random.uniform(key_of[2], (CHANNELS,), jnp.float32, 0.5, 1.5), 0.5, 1.5)
    out_grad = normal_values(key_of[3], (LENGTH, CHANNELS), 1.0, 6.0, ((0, 128),))
    return dict(signal=signal, filter_param=filter_param, skip_gain=skip_gain, out_grad=out_grad)


def reference(signal, filter_param, skip_gain, out_grad):
    scale = 1.0 / math.sqrt(LENGTH)
    filt_spec = jnp.fft.fft(filter_param.astype(jnp.float32), axis=0) * scale
    values = signal.astype(jnp.float32)
    cotan = out_grad.astype(jnp.float32)
    sig_spec = jnp.fft.fft(values, axis=0)
    grad_spec = jnp.fft.fft(cotan, axis=0)
    conv = jnp.real(jnp.fft.ifft(sig_spec * filt_spec, axis=0)) + skip_gain * values
    back = jnp.real(jnp.fft.ifft(jnp.conj(filt_spec) * grad_spec, axis=0)) + skip_gain * cotan
    taps = jnp.real(jnp.fft.ifft(jnp.conj(sig_spec) * grad_spec, axis=0)) * scale
    return (conv.astype(jnp.bfloat16), back.astype(jnp.bfloat16), taps.astype(jnp.float32))
```

```python
import math

import numpy as np

import jax
import jax.numpy as jnp
from jax import lax
from jax.sharding import PartitionSpec as P

FIRST_LEN = 512
AXES = ("seq", "dp")

highest = lax.Precision.HIGHEST


def half_table(order):
    half = order // 2
    slot = np.arange(half)[:, None]
    pos = np.arange(order)[None, :]
    angle = (slot * pos % order) * (2.0 * np.pi / order)
    real_rows = np.cos(angle)
    imag_rows = -np.sin(angle)
    real_rows[0, :] = 1.0
    imag_rows[0, :] = np.where(np.arange(order) % 2 == 0, 1.0, -1.0)
    return jnp.asarray(np.concatenate([real_rows, imag_rows], axis=0), dtype=jnp.float32)


def full_table(order):
    idx = np.arange(order)
    angle = (idx[:, None] * idx[None, :] % order) * (2.0 * np.pi / order)
    c, s = np.cos(angle), np.sin(angle)
    top = np.concatenate([c, s], axis=1)
    bottom = np.concatenate([-s, c], axis=1)
    return jnp.asarray(np.concatenate([top, bottom], axis=0), dtype=jnp.float32)


def rotate(re, im, cos_t, sin_t):
    return re * cos_t - im * sin_t, re * sin_t + im * cos_t


def per_device(signal, filter_param, skip_gain, out_grad):
    dev_count = lax.axis_size(AXES)
    me = lax.axis_index(AXES)
    tok_rows, chans = signal.shape
    length = tok_rows * dev_count
    first_len = FIRST_LEN
    second_len = length // first_len
    first_dev = first_len // dev_count
    half = first_len // 2
    slots = half // dev_count
    assert second_len == dev_count and slots * dev_count == half

    stacked = jnp.concatenate([signal, out_grad, filter_param], axis=1)
    blocks = stacked.reshape(first_dev, second_len, 3 * chans)
    columns = lax.all_to_all(blocks, AXES, split_axis=1, concat_axis=0, tiled=True)
    columns = columns.reshape(first_len, 3 * chans).astype(jnp.float32)

    table_a = half_table(first_len)
    part = jnp.dot(table_a, columns, precision=highest)
    part = part.reshape(2, dev_count, slots, 3 * chans)

    got = lax.all_to_all(part, AXES, split_axis=1, concat_axis=1, tiled=True)
    z_re, z_im = got[0], got[1]

    pos_b = jnp.arange(second_len, dtype=jnp.float32)[:, None]
    freq = (me * slots + jnp.arange(slots, dtype=jnp.int32)).astype(jnp.float32)[None, :]
    phase = pos_b * freq * (-2.0 * math.pi / length)
    tw_c = jnp.cos(phase)[:, :, None]
    tw_s = jnp.sin(phase)[:, :, None]
    t_re, t_im = rotate(z_re, z_im, tw_c, tw_s)
    is_first = me == 0
    t_im0 = jnp.where(is_first, 0.0, t_im[:, 0:1])
    nyq_phase = pos_b * (-2.0 * math.pi * half / length)
    nyq_c = jnp.cos(nyq_phase)[:, :, None]
    nyq_s = jnp.sin(nyq_phase)[:, :, None]
    extra_re = jnp.where(is_first, z_im[:, 0:1] * nyq_c, 0.0)
    extra_im = jnp.where(is_first, z_im[:, 0:1] * nyq_s, 0.0)
    rows_re = jnp.concatenate([t_re, extra_re], axis=1)
    rows_im = jnp.concatenate([t_im0, t_im[:, 1:], extra_im], axis=1)
    nrows = slots + 1

    table_b = full_table(second_len)
    both = jnp.stack([rows_re, rows_im]).reshape(2 * second_len, nrows * 3 * chans)
    spec = jnp.dot(table_b, both, precision=highest).reshape(2, second_len, nrows, 3 * chans)
    sr, si = spec[0], spec[1]
    sig_r, cot_r, flt_r = sr[..., :chans], sr[..., chans : 2 * chans], sr[..., 2 * chans :]
    sig_i, cot_i, flt_i = si[..., :chans], si[..., chans : 2 * chans], si[..., 2 * chans :]

    scale = 1.0 / (math.sqrt(length) * length)
    conv_r = (sig_r * flt_r - sig_i * flt_i) * scale
    conv_i = (sig_r * flt_i + sig_i * flt_r) * scale
    back_r = (flt_r * cot_r + flt_i * cot_i) * scale
    back_i = (flt_r * cot_i - flt_i * cot_r) * scale
    taps_r = (sig_r * cot_r + sig_i * cot_i) * scale
    taps_i = (sig_r * cot_i - sig_i * cot_r) * scale
    prod = jnp.stack(
        [
            jnp.concatenate([conv_r, back_r, taps_r], axis=-1),
            jnp.concatenate([conv_i, back_i, taps_i], axis=-1),
        ]
    ).reshape(2 * second_len, nrows * 3 * chans)

    unit = lax.dot_general(
        table_b, prod, (((0,), (0,)), ((), ())), precision=highest
    ).reshape(2, second_len, nrows, 3 * chans)
    u_re, u_im = unit[0], unit[1]
    v_re, v_im = rotate(u_re[:, :slots], u_im[:, :slots], tw_c, -tw_s)
    x_re, _ = rotate(u_re[:, slots:], u_im[:, slots:], nyq_c, -nyq_s)
    out_re0 = jnp.where(is_first, v_re[:, 0:1], 2.0 * v_re[:, 0:1])
    out_im0 = jnp.where(is_first, x_re, 2.0 * v_im[:, 0:1])
    out_re = jnp.concatenate([out_re0, 2.0 * v_re[:, 1:]], axis=1)
    out_im = jnp.concatenate([out_im0, 2.0 * v_im[:, 1:]], axis=1)
    back_part = jnp.stack([out_re, out_im])

    ret = lax.all_to_all(back_part, AXES, split_axis=1, concat_axis=1, tiled=True)
    ret = ret.reshape(first_len, 3 * chans)

    times = lax.dot_general(table_a, ret, (((0,), (0,)), ((), ())), precision=highest)
    conv_cols = times[:, :chans] + skip_gain * columns[:, :chans]
    back_cols = times[:, chans : 2 * chans] + skip_gain * columns[:, chans : 2 * chans]
    taps_cols = times[:, 2 * chans :]
    taps_hi = lax.reduce_precision(taps_cols, exponent_bits=8, mantissa_bits=7)
    taps_lo = taps_cols - taps_hi
    outs = jnp.concatenate(
        [
            conv_cols.astype(jnp.bfloat16),
            back_cols.astype(jnp.bfloat16),
            taps_hi.astype(jnp.bfloat16),
            taps_lo.astype(jnp.bfloat16),
        ],
        axis=1,
    ).reshape(dev_count, first_dev, 1, 4 * chans)

    rows = lax.all_to_all(outs, AXES, split_axis=0, concat_axis=2, tiled=True)
    rows = rows.reshape(tok_rows, 4 * chans)
    conv_out = rows[:, :chans]
    input_grad = rows[:, chans : 2 * chans]
    filter_grad = rows[:, 2 * chans : 3 * chans].astype(jnp.float32) + rows[:, 3 * chans :].astype(
        jnp.float32
    )
    return (conv_out, input_grad, filter_grad)


def solution(mesh):
    placed = (P(AXES, None), P(AXES, None), P(), P(AXES, None))
    return jax.shard_map(
        per_device,
        mesh=mesh,
        in_specs=placed,
        out_specs=(P(AXES, None), P(AXES, None), P(AXES, None)),
        check_vma=False,
    )
```

```python
import math

import numpy as np

import jax
import jax.numpy as jnp
from jax import lax
from jax.sharding import PartitionSpec as P

AXES = ("seq", "dp")

highest = lax.Precision.HIGHEST


def half_table(order):
    half = order // 2
    slot = np.arange(half)[:, None]
    pos = np.arange(order)[None, :]
    angle = (slot * pos % order) * (2.0 * np.pi / order)
    real_rows = np.cos(angle)
    imag_rows = -np.sin(angle)
    real_rows[0, :] = 1.0
    imag_rows[0, :] = np.where(np.arange(order) % 2 == 0, 1.0, -1.0)
    return jnp.asarray(np.concatenate([real_rows, imag_rows], axis=0), dtype=jnp.float32)


def pair_table(order):
    idx = np.arange(order)
    angle = (idx[:, None] * idx[None, :] % order) * (2.0 * np.pi / order)
    return jnp.asarray(np.concatenate([np.cos(angle), np.sin(angle)], axis=1), dtype=jnp.float32)


def twiddle(rows, cols, length):
    k = np.arange(rows)[:, None]
    n = np.arange(cols)[None, :]
    angle = (k * n % length) * (-2.0 * np.pi / length)
    return (
        jnp.asarray(np.cos(angle), dtype=jnp.float32),
        jnp.asarray(np.sin(angle), dtype=jnp.float32),
    )


def rotate(re, im, cos_t, sin_t):
    return re * cos_t - im * sin_t, re * sin_t + im * cos_t


def per_device(signal, filter_param, skip_gain, out_grad):
    dev_count = lax.axis_size(AXES)
    me = lax.axis_index(AXES)
    tok_rows, chans = signal.shape
    length = tok_rows * dev_count
    side = math.isqrt(length)
    half = side // 2
    assert chans == dev_count and side * side == length

    stacked = jnp.stack([signal, out_grad, filter_param], axis=0)
    send = jnp.transpose(stacked, (2, 0, 1))
    got = lax.all_to_all(send, AXES, split_axis=0, concat_axis=2, tiled=True)
    seqs = got.reshape(3, side, side).astype(jnp.float32)

    table_a = half_table(side)
    part = jnp.einsum("kn,anm->akm", table_a, seqs, precision=highest)
    y_re, y_im = part[:, :half], part[:, half:]
    zero_row = jnp.zeros((3, 1, side), jnp.float32)
    rows_re = jnp.concatenate([y_re, y_im[:, 0:1]], axis=1)
    rows_im = jnp.concatenate([zero_row, y_im[:, 1:], zero_row], axis=1)
    tw_c, tw_s = twiddle(half + 1, side, length)
    t_re, t_im = rotate(rows_re, rows_im, tw_c, tw_s)

    table_b = pair_table(side)
    both = jnp.concatenate([t_re, t_im], axis=0)
    prod_b = jnp.einsum("akn,nm->akm", both, table_b, precision=highest)
    cc, cs = prod_b[..., :side], prod_b[..., side:]
    s_re = cc[:3] + cs[3:]
    s_im = cc[3:] - cs[:3]
    sig_r, cot_r, flt_r = s_re[0], s_re[1], s_re[2]
    sig_i, cot_i, flt_i = s_im[0], s_im[1], s_im[2]

    scale = 1.0 / (math.sqrt(length) * length)
    p_re = jnp.stack(
        [
            sig_r * flt_r - sig_i * flt_i,
            flt_r * cot_r + flt_i * cot_i,
            sig_r * cot_r + sig_i * cot_i,
        ]
    ) * scale
    p_im = jnp.stack(
        [
            sig_r * flt_i + sig_i * flt_r,
            flt_r * cot_i - flt_i * cot_r,
            sig_r * cot_i - sig_i * cot_r,
        ]
    ) * scale

    both = jnp.concatenate([p_re, p_im], axis=0)
    prod_b = jnp.einsum("akn,nm->akm", both, table_b, precision=highest)
    cc, cs = prod_b[..., :side], prod_b[..., side:]
    u_re = cc[:3] - cs[3:]
    u_im = cc[3:] + cs[:3]
    v_re, v_im = rotate(u_re, u_im, tw_c, -tw_s)

    pack_re = jnp.concatenate([v_re[:, 0:1], 2.0 * v_re[:, 1:half]], axis=1)
    pack_im = jnp.concatenate([v_re[:, half:], 2.0 * v_im[:, 1:half]], axis=1)
    packed = jnp.concatenate([pack_re, pack_im], axis=1)
    times = jnp.einsum("sn,asm->anm", table_a, packed, precision=highest).reshape(3, length)

    gain = lax.dynamic_index_in_dim(skip_gain, me, keepdims=False)
    flat = seqs.reshape(3, length)
    conv = times[0] + gain * flat[0]
    back = times[1] + gain * flat[1]
    taps = times[2]
    taps_hi = lax.reduce_precision(taps, exponent_bits=8, mantissa_bits=7)
    taps_lo = taps - taps_hi
    outs = jnp.stack(
        [
            conv.astype(jnp.bfloat16),
            back.astype(jnp.bfloat16),
            taps_hi.astype(jnp.bfloat16),
            taps_lo.astype(jnp.bfloat16),
        ]
    ).reshape(4, dev_count, tok_rows)

    rows = lax.all_to_all(outs, AXES, split_axis=1, concat_axis=1, tiled=True)
    rows = jnp.transpose(rows, (0, 2, 1))
    conv_out = rows[0]
    input_grad = rows[1]
    filter_grad = rows[2].astype(jnp.float32) + rows[3].astype(jnp.float32)
    return (conv_out, input_grad, filter_grad)


def solution(mesh):
    placed = (P(AXES, None), P(AXES, None), P(), P(AXES, None))
    return jax.shard_map(
        per_device,
        mesh=mesh,
        in_specs=placed,
        out_specs=(P(AXES, None), P(AXES, None), P(AXES, None)),
        check_vma=False,
    )
```

```python
import math

import numpy as np

import jax
import jax.numpy as jnp
from jax import lax
from jax.sharding import PartitionSpec as P

AXES = ("seq", "dp")

matmul_precision = lax.Precision.HIGH


def half_table(order):
    half = order // 2
    slot = np.arange(half)[:, None]
    pos = np.arange(order)[None, :]
    angle = (slot * pos % order) * (2.0 * np.pi / order)
    real_rows = np.cos(angle)
    imag_rows = -np.sin(angle)
    real_rows[0, :] = 1.0
    imag_rows[0, :] = np.where(np.arange(order) % 2 == 0, 1.0, -1.0)
    return jnp.asarray(np.concatenate([real_rows, imag_rows], axis=0), dtype=jnp.float32)


def pair_table(order):
    idx = np.arange(order)
    angle = (idx[:, None] * idx[None, :] % order) * (2.0 * np.pi / order)
    return jnp.asarray(np.concatenate([np.cos(angle), np.sin(angle)], axis=1), dtype=jnp.float32)


def twiddle(rows, cols, length):
    k = np.arange(rows)[:, None]
    n = np.arange(cols)[None, :]
    angle = (k * n % length) * (-2.0 * np.pi / length)
    return (
        jnp.asarray(np.cos(angle), dtype=jnp.float32),
        jnp.asarray(np.sin(angle), dtype=jnp.float32),
    )


def rotate(re, im, cos_t, sin_t):
    return re * cos_t - im * sin_t, re * sin_t + im * cos_t


def per_device(signal, filter_param, skip_gain, out_grad):
    dev_count = lax.axis_size(AXES)
    me = lax.axis_index(AXES)
    tok_rows, chans = signal.shape
    length = tok_rows * dev_count
    side = math.isqrt(length)
    half = side // 2
    assert chans == dev_count and side * side == length

    stacked = jnp.stack([signal, out_grad, filter_param], axis=0)
    send = jnp.transpose(stacked, (2, 0, 1))
    got = lax.all_to_all(send, AXES, split_axis=0, concat_axis=2, tiled=True)
    seqs = got.reshape(3, side, side).astype(jnp.float32)

    table_a = half_table(side)
    part = jnp.einsum("kn,anm->akm", table_a, seqs, precision=matmul_precision)
    y_re, y_im = part[:, :half], part[:, half:]
    zero_row = jnp.zeros((3, 1, side), jnp.float32)
    rows_re = jnp.concatenate([y_re, y_im[:, 0:1]], axis=1)
    rows_im = jnp.concatenate([zero_row, y_im[:, 1:], zero_row], axis=1)
    tw_c, tw_s = twiddle(half + 1, side, length)
    t_re, t_im = rotate(rows_re, rows_im, tw_c, tw_s)

    table_b = pair_table(side)
    both = jnp.concatenate([t_re, t_im], axis=0)
    prod_b = jnp.einsum("akn,nm->akm", both, table_b, precision=matmul_precision)
    cc, cs = prod_b[..., :side], prod_b[..., side:]
    s_re = cc[:3] + cs[3:]
    s_im = cc[3:] - cs[:3]
    sig_r, cot_r, flt_r = s_re[0], s_re[1], s_re[2]
    sig_i, cot_i, flt_i = s_im[0], s_im[1], s_im[2]

    scale = 1.0 / (math.sqrt(length) * length)
    p_re = jnp.stack(
        [
            sig_r * flt_r - sig_i * flt_i,
            flt_r * cot_r + flt_i * cot_i,
            sig_r * cot_r + sig_i * cot_i,
        ]
    ) * scale
    p_im = jnp.stack(
        [
            sig_r * flt_i + sig_i * flt_r,
            flt_r * cot_i - flt_i * cot_r,
            sig_r * cot_i - sig_i * cot_r,
        ]
    ) * scale

    both = jnp.concatenate([p_re, p_im], axis=0)
    prod_b = jnp.einsum("akn,nm->akm", both, table_b, precision=matmul_precision)
    cc, cs = prod_b[..., :side], prod_b[..., side:]
    u_re = cc[:3] - cs[3:]
    u_im = cc[3:] + cs[:3]
    v_re, v_im = rotate(u_re, u_im, tw_c, -tw_s)

    pack_re = jnp.concatenate([v_re[:, 0:1], 2.0 * v_re[:, 1:half]], axis=1)
    pack_im = jnp.concatenate([v_re[:, half:], 2.0 * v_im[:, 1:half]], axis=1)
    packed = jnp.concatenate([pack_re, pack_im], axis=1)
    times = jnp.einsum("sn,asm->anm", table_a, packed, precision=matmul_precision).reshape(3, length)

    gain = lax.dynamic_index_in_dim(skip_gain, me, keepdims=False)
    flat = seqs.reshape(3, length)
    conv = times[0] + gain * flat[0]
    back = times[1] + gain * flat[1]
    taps = times[2]
    taps_hi = lax.reduce_precision(taps, exponent_bits=8, mantissa_bits=7)
    taps_lo = taps - taps_hi
    outs = jnp.stack(
        [
            conv.astype(jnp.bfloat16),
            back.astype(jnp.bfloat16),
            taps_hi.astype(jnp.bfloat16),
            taps_lo.astype(jnp.bfloat16),
        ]
    ).reshape(4, dev_count, tok_rows)

    rows = lax.all_to_all(outs, AXES, split_axis=1, concat_axis=1, tiled=True)
    rows = jnp.transpose(rows, (0, 2, 1))
    conv_out = rows[0]
    input_grad = rows[1]
    filter_grad = rows[2].astype(jnp.float32) + rows[3].astype(jnp.float32)
    return (conv_out, input_grad, filter_grad)


def solution(mesh):
    placed = (P(AXES, None), P(AXES, None), P(), P(AXES, None))
    return jax.shard_map(
        per_device,
        mesh=mesh,
        in_specs=placed,
        out_specs=(P(AXES, None), P(AXES, None), P(AXES, None)),
        check_vma=False,
    )
```

```python
import math

import numpy as np

import jax
import jax.numpy as jnp
from jax import lax
from jax.sharding import PartitionSpec as P

AXES = ("seq", "dp")

matmul_precision = lax.Precision.HIGH


def half_table(order):
    half = order // 2
    slot = np.arange(half)[:, None]
    pos = np.arange(order)[None, :]
    angle = (slot * pos % order) * (2.0 * np.pi / order)
    real_rows = np.cos(angle)
    imag_rows = -np.sin(angle)
    real_rows[0, :] = 1.0
    imag_rows[0, :] = np.where(np.arange(order) % 2 == 0, 1.0, -1.0)
    return jnp.asarray(np.concatenate([real_rows, imag_rows], axis=0), dtype=jnp.float32)


def pair_table(order):
    idx = np.arange(order)
    angle = (idx[:, None] * idx[None, :] % order) * (2.0 * np.pi / order)
    return jnp.asarray(np.concatenate([np.cos(angle), np.sin(angle)], axis=1), dtype=jnp.float32)


def twiddle(rows, cols, length):
    k = np.arange(rows)[:, None]
    n = np.arange(cols)[None, :]
    angle = (k * n % length) * (-2.0 * np.pi / length)
    return (
        jnp.asarray(np.cos(angle), dtype=jnp.float32),
        jnp.asarray(np.sin(angle), dtype=jnp.float32),
    )


def rotate(re, im, cos_t, sin_t):
    return re * cos_t - im * sin_t, re * sin_t + im * cos_t


def per_device(signal, filter_param, skip_gain, out_grad):
    dev_count = lax.axis_size(AXES)
    me = lax.axis_index(AXES)
    tok_rows, chans = signal.shape
    length = tok_rows * dev_count
    side = math.isqrt(length)
    half = side // 2
    assert chans == dev_count and side * side == length

    stacked = jnp.stack([signal, out_grad, filter_param], axis=0)
    send = jnp.transpose(stacked, (2, 0, 1)).reshape(dev_count, 4, 3 * tok_rows // 4)
    got = lax.all_to_all(send, AXES, split_axis=0, concat_axis=0, tiled=True)
    got = jnp.transpose(got.reshape(dev_count, 3, tok_rows), (1, 0, 2))
    seqs = got.reshape(3, side, side).astype(jnp.float32)

    table_a = half_table(side)
    part = jnp.einsum("kn,anm->akm", table_a, seqs, precision=matmul_precision)
    y_re, y_im = part[:, :half], part[:, half:]
    zero_row = jnp.zeros((3, 1, side), jnp.float32)
    rows_re = jnp.concatenate([y_re, y_im[:, 0:1]], axis=1)
    rows_im = jnp.concatenate([zero_row, y_im[:, 1:], zero_row], axis=1)
    tw_c, tw_s = twiddle(half + 1, side, length)
    t_re, t_im = rotate(rows_re, rows_im, tw_c, tw_s)

    table_b = pair_table(side)
    both = jnp.concatenate([t_re, t_im], axis=0)
    prod_b = jnp.einsum("akn,nm->akm", both, table_b, precision=matmul_precision)
    cc, cs = prod_b[..., :side], prod_b[..., side:]
    s_re = cc[:3] + cs[3:]
    s_im = cc[3:] - cs[:3]
    sig_r, cot_r, flt_r = s_re[0], s_re[1], s_re[2]
    sig_i, cot_i, flt_i = s_im[0], s_im[1], s_im[2]

    scale = 1.0 / (math.sqrt(length) * length)
    p_re = jnp.stack(
        [
            sig_r * flt_r - sig_i * flt_i,
            flt_r * cot_r + flt_i * cot_i,
            sig_r * cot_r + sig_i * cot_i,
        ]
    ) * scale
    p_im = jnp.stack(
        [
            sig_r * flt_i + sig_i * flt_r,
            flt_r * cot_i - flt_i * cot_r,
            sig_r * cot_i - sig_i * cot_r,
        ]
    ) * scale

    both = jnp.concatenate([p_re, p_im], axis=0)
    prod_b = jnp.einsum("akn,nm->akm", both, table_b, precision=matmul_precision)
    cc, cs = prod_b[..., :side], prod_b[..., side:]
    u_re = cc[:3] - cs[3:]
    u_im = cc[3:] + cs[:3]
    v_re, v_im = rotate(u_re, u_im, tw_c, -tw_s)

    pack_re = jnp.concatenate([v_re[:, 0:1], 2.0 * v_re[:, 1:half]], axis=1)
    pack_im = jnp.concatenate([v_re[:, half:], 2.0 * v_im[:, 1:half]], axis=1)
    packed = jnp.concatenate([pack_re, pack_im], axis=1)
    times = jnp.einsum("sn,asm->anm", table_a, packed, precision=matmul_precision).reshape(3, length)

    gain = lax.dynamic_index_in_dim(skip_gain, me, keepdims=False)
    flat = seqs.reshape(3, length)
    conv = times[0] + gain * flat[0]
    back = times[1] + gain * flat[1]
    taps = times[2]
    taps_hi = lax.reduce_precision(taps, exponent_bits=8, mantissa_bits=7)
    taps_lo = taps - taps_hi
    outs = jnp.stack(
        [
            conv.astype(jnp.bfloat16),
            back.astype(jnp.bfloat16),
            taps_hi.astype(jnp.bfloat16),
            taps_lo.astype(jnp.bfloat16),
        ]
    ).reshape(4, dev_count, tok_rows)

    rows = lax.all_to_all(outs, AXES, split_axis=1, concat_axis=1, tiled=True)
    rows = jnp.transpose(rows, (0, 2, 1))
    conv_out = rows[0]
    input_grad = rows[1]
    filter_grad = rows[2].astype(jnp.float32) + rows[3].astype(jnp.float32)
    return (conv_out, input_grad, filter_grad)


def solution(mesh):
    placed = (P(AXES, None), P(AXES, None), P(), P(AXES, None))
    return jax.shard_map(
        per_device,
        mesh=mesh,
        in_specs=placed,
        out_specs=(P(AXES, None), P(AXES, None), P(AXES, None)),
        check_vma=False,
    )
```
